512 devices in a mesh: seq: 128 (over y, z, core), head: 4 (over x).
Axes of the slice: x: 4, y: 8, z: 8, core: 2. Of those that a mesh axis runs over, the one named last changes fastest.
Arguments:
- x_raw: bfloat16 [32768, 4096], P('seq', 'head'), may hold values from -6 to 6
- bc_raw: bfloat16 [32768, 256], P('seq'), may hold values from -6 to 6
- gate_z: bfloat16 [32768, 4096], P('seq', 'head'), may hold values from -6 to 6
- step_size: float32 [32768, 64], P('seq', 'head'), may hold values from 0.002 to 0.05
- log_decay: float32 [32768, 64], P('seq', 'head'), may hold values from -1 to 0, as said below
- doc_ids: int32 [32768], P('seq'), may hold values from 0 to 63, as said below
- conv_x: float32 [4, 4096], P(None, 'head'), may hold values from -3 to 3
- conv_bc: float32 [4, 256], replicated, may hold values from -3 to 3
- skip: float32 [64], P('head'), may hold values from 0.5 to 2
- norm_gain: float32 [4096], P('head'), may hold values from 0.25 to 1.75
Outputs:
- mixed: bfloat16 [32768, 4096], P('seq', 'head')
The draws below stay inside these ranges and needn't reach their ends.
Inputs may be any that keep to these rules, and one draw needn't show every extreme that they name: `doc_ids`: document ids never fall along the sequence; each document has 1 to 4096 tokens, one exactly 4096. `log_decay`: every entry is negative.
All inputs are finite; a program needn't handle non-finite values.
Results may differ from the reference program's by a relative error of at most 0.005.
Values may be sent and summed in bfloat16 or wider, within the bound.
No kernel may reach another device: no remote copies, remote signals or barrier semaphores. Data moves between devices by JAX's collectives and lax.ppermute only.
A program may use at most 192 MiB of HBM per device.

```python
import jax
import jax.numpy as jnp
from jax import lax

H = 64
P_SIZE = 64
N = 128
GROUP = 256
KW = 4
TOK_DEV = 256
JOINED_ITEMS = 32768
MAX_TEXT_SPAN = 4096
DOCS = 64


def text_layout(key):
    sampler_seeds = jax.random.split(jax.random.fold_in(key, 29), 3)
    remaining = JOINED_ITEMS - MAX_TEXT_SPAN
    pieces = DOCS - 1
    weights = jax.random.randint(sampler_seeds[0], (pieces,), 1, 4).astype(jnp.int32)
    running = jnp.cumsum(weights).astype(jnp.int32)
    boundaries = (remaining * running[:-1] // running[-1]).astype(jnp.int32)
    first_dev = jax.random.randint(sampler_seeds[1], (), 0, remaining // TOK_DEV).astype(jnp.int32)
    offset = jax.random.randint(sampler_seeds[2], (), TOK_DEV // 4, 3 * TOK_DEV // 4 + 1).astype(jnp.int32)
    doc_start = first_dev * TOK_DEV + offset
    nearest = jnp.argmin(jnp.abs(boundaries - doc_start))
    placed = jnp.where(jnp.arange(pieces - 1) == nearest, doc_start, boundaries)
    placed = jnp.sort(placed).astype(jnp.int32)
    return (doc_start, placed)


def draw_doc_ids(key, part):
    doc_start, placed = text_layout(key)
    positions = jnp.arange(JOINED_ITEMS, dtype=jnp.int32)
    line_index = jnp.where(positions < doc_start, positions, positions - MAX_TEXT_SPAN)
    counted = jnp.sum((placed[None, :] <= line_index[:, None]).astype(jnp.int32), axis=1)
    inside = (positions >= doc_start) & (positions < doc_start + MAX_TEXT_SPAN)
    after_long = (positions >= doc_start + MAX_TEXT_SPAN).astype(jnp.int32)
    long_id = jnp.sum((placed < doc_start).astype(jnp.int32)) + 1
    return jnp.where(inside, long_id, counted + after_long).astype(jnp.int32)


def draw_step_size(key, part):
    doc_start, placed = text_layout(key)
    sampler_seeds = jax.random.split(jax.random.fold_in(key, 13), 3)
    spread_rate = jnp.exp(jax.random.uniform(sampler_seeds[0], (JOINED_ITEMS, H), jnp.float32, jnp.log(0.00505), jnp.log(0.0495)))
    early_rate = jax.random.uniform(sampler_seeds[1], (JOINED_ITEMS, H), jnp.float32, 0.04, 0.05)
    late_rate = jax.random.uniform(sampler_seeds[2], (JOINED_ITEMS, H), jnp.float32, 0.002, 0.003)
    relative = jnp.arange(JOINED_ITEMS, dtype=jnp.int32) - doc_start
    early = (relative >= 0) & (relative < MAX_TEXT_SPAN // 8)
    later = (relative >= MAX_TEXT_SPAN // 8) & (relative < MAX_TEXT_SPAN)
    return jnp.where(early[:, None], early_rate, jnp.where(later[:, None], late_rate, spread_rate))


def draw_x_raw(key, part):
    doc_start, placed = text_layout(key)
    sampler_seeds = jax.random.split(jax.random.fold_in(key, 17), 1)
    values = jnp.clip(jax.random.normal(sampler_seeds[0], (JOINED_ITEMS, H * P_SIZE), jnp.float32), -6.0, 6.0)
    relative = jnp.arange(JOINED_ITEMS, dtype=jnp.int32) - doc_start
    quiet = (relative >= MAX_TEXT_SPAN - 3 * MAX_TEXT_SPAN // 16) & (relative < MAX_TEXT_SPAN)
    return (values * jnp.where(quiet, 0.05, 1.0)[:, None]).astype(jnp.bfloat16)


def draw_log_decay(key, part):
    sampler_seeds = jax.random.split(jax.random.fold_in(key, 11), 6)
    fast_share = 0.5
    fast_heads = jax.random.bernoulli(sampler_seeds[0], fast_share, (H,))
    slow_rate = jnp.exp(jax.random.uniform(sampler_seeds[1], (H,), jnp.float32, jnp.log(0.02), jnp.log(0.3))) / MAX_TEXT_SPAN
    fast_rate = jax.random.uniform(sampler_seeds[2], (H,), jnp.float32, 1.0 / 50.0, 1.0 / 30.0)
    forgetting_speed = jnp.where(fast_heads, fast_rate, slow_rate)
    multiplier_amplitude = jax.random.uniform(sampler_seeds[3], (JOINED_ITEMS, H), jnp.float32, 0.5, 2.0)
    contiguous_run_size = jax.random.bernoulli(sampler_seeds[4], 2.0 / MAX_TEXT_SPAN, (JOINED_ITEMS, 1)).astype(jnp.float32)
    stacked_level_index = jax.random.uniform(sampler_seeds[5], (JOINED_ITEMS, 1), jnp.float32, 0.2, 0.7)
    return -(forgetting_speed[None, :] * multiplier_amplitude) - contiguous_run_size * stacked_level_index


def steps_of(stream_key, dims, cuts, low, top_value):
    factor_of = 1.0
    for axis_at, blocks in cuts:
        heights = jax.random.uniform(jax.random.fold_in(jax.random.fold_in(stream_key, 6), axis_at), (blocks,), jnp.float32, low / len(cuts), top_value / len(cuts))
        factor_of = factor_of * jnp.repeat(jnp.exp(heights), dims[axis_at] // blocks).reshape((-1,) + (1,) * (len(dims) - 1 - axis_at))
    return factor_of


def normal_values(key, shape, spread, bound, cuts=(), kind=jnp.bfloat16):
    values = jax.random.normal(key, shape, jnp.float32) * spread
    if len(cuts) > 0:
        values = steps_of(key, shape, cuts, -0.22, 0.18) * values
    return jnp.clip(values, min=-bound, max=bound).astype(kind)


def setup_inputs(seed: int = 0) -> dict:
    seeds = jax.random.split(jax.random.key(seed), 11)
    x_raw = draw_x_raw(jax.random.fold_in(seeds[10], 71), 0)
    bc_raw = normal_values(seeds[1], (JOINED_ITEMS, 2 * N), 1.0, 6.0, ((0, 128),))
    gate_z = normal_values(seeds[2], (JOINED_ITEMS, H * P_SIZE), 1.0, 6.0, ((0, 128), (1, 4)))
    step_size = draw_step_size(jax.random.fold_in(seeds[10], 71), 0)
    log_decay = draw_log_decay(jax.random.fold_in(seeds[10], 71), 0)
    doc_ids = draw_doc_ids(jax.random.fold_in(seeds[10], 71), 0)
    conv_x = normal_values(seeds[6], (KW, H * P_SIZE), KW ** -0.5, 3.0, ((1, 4),), jnp.float32)
    conv_bc = normal_values(seeds[7], (KW, 2 * N), KW ** -0.5, 3.0, (), jnp.float32)
    skip = jnp.clip(0.5 + 1.5 * jax.random.uniform(seeds[8], (H,), jnp.float32) ** steps_of(seeds[8], (H,), ((0, 4),), -0.2, 0.2), 0.5, 2.0)
    norm_gain = jnp.clip(1.0 + 0.15 * jax.random.normal(seeds[9], (H * P_SIZE,), jnp.float32), 0.25, 1.75)
    return dict(x_raw=x_raw, bc_raw=bc_raw, gate_z=gate_z, step_size=step_size, log_decay=log_decay, doc_ids=doc_ids, conv_x=conv_x, conv_bc=conv_bc, skip=skip, norm_gain=norm_gain)


EPS = 1e-05

def conv_silu(raw, weight, doc_ids):
    rows = raw.shape[0]
    values = raw.astype(jnp.float32)
    total = jnp.zeros(raw.shape, jnp.float32)
    for k in range(KW):
        moved = jnp.concatenate([jnp.zeros((k, raw.shape[1]), jnp.float32), values[:rows - k]], axis=0)
        earlier = jnp.concatenate([jnp.full((k,), -1, jnp.int32), doc_ids[:rows - k]], axis=0)
        keep = (earlier == doc_ids).astype(jnp.float32)
        total = total + weight[k][None, :] * moved * keep[:, None]
    return lax.optimization_barrier(jax.nn.silu(total).astype(jnp.bfloat16))

def reference(x_raw, bc_raw, gate_z, step_size, log_decay, doc_ids, conv_x, conv_bc, skip, norm_gain):
    xconv = conv_silu(x_raw, conv_x, doc_ids)
    bconv = conv_silu(bc_raw, conv_bc, doc_ids)
    blocks = JOINED_ITEMS // GROUP
    xdt = (xconv.astype(jnp.float32).reshape(JOINED_ITEMS, H, P_SIZE) * step_size[:, :, None]).astype(jnp.bfloat16)
    xdt = lax.optimization_barrier(xdt)
    pieces = (xconv.reshape(blocks, GROUP, H, P_SIZE), xdt.reshape(blocks, GROUP, H, P_SIZE), bconv[:, :N].reshape(blocks, GROUP, N), bconv[:, N:].reshape(blocks, GROUP, N), gate_z.reshape(blocks, GROUP, H * P_SIZE), log_decay.reshape(blocks, GROUP, H), doc_ids.reshape(blocks, GROUP))
    lower = jnp.arange(GROUP)[:, None] >= jnp.arange(GROUP)[None, :]

    def block_step(carry, piece):
        state, prev_id = carry
        xs, xin, bmat, cmat, zs, decay, ids = piece
        cum = jnp.cumsum(decay, axis=0)
        gram = jnp.dot(cmat, bmat.T, preferred_element_type=jnp.float32)
        mask = ((ids[:, None] == ids[None, :]) & lower)[None]
        diff = cum.T[:, :, None] - cum.T[:, None, :]
        weights = jnp.where(mask, jnp.exp(jnp.where(mask, diff, 0.0)), 0.0) * gram[None]
        weights = lax.optimization_barrier(weights.astype(jnp.bfloat16))
        inner = jnp.einsum('hts,shp->thp', weights.astype(jnp.float32), xin.astype(jnp.float32))
        cont = (ids == prev_id).astype(jnp.float32)
        entry = jnp.exp(cum) * cont[:, None]
        entered = lax.optimization_barrier(state.astype(jnp.bfloat16))
        carried = jnp.einsum('tn,hpn->thp', cmat.astype(jnp.float32), entered.astype(jnp.float32)) * entry[:, :, None]
        scanned = inner + carried + skip[None, :, None] * xs.astype(jnp.float32)
        gated = scanned.reshape(GROUP, H * P_SIZE) * jax.nn.silu(zs.astype(jnp.float32))
        scale = lax.rsqrt(lax.optimization_barrier(jnp.sum(gated * gated, axis=1)) / (H * P_SIZE) + EPS)
        result = (gated * scale[:, None] * norm_gain[None, :]).astype(jnp.bfloat16)
        ends = jnp.where((ids == ids[-1])[:, None], jnp.exp(cum[-1][None, :] - cum), 0.0)
        written = lax.optimization_barrier((xin.astype(jnp.float32) * ends[:, :, None]).astype(jnp.bfloat16))
        local = jnp.einsum('shp,sn->hpn', written.astype(jnp.float32), bmat.astype(jnp.float32))
        through = jnp.exp(cum[-1]) * cont[-1]
        state = through[:, None, None] * state + local
        return ((state, ids[-1]), result)
    start = (jnp.zeros((H, P_SIZE, N), jnp.float32), jnp.array(-1, jnp.int32))
    final, results = lax.scan(block_step, start, pieces)
    return results.reshape(JOINED_ITEMS, H * P_SIZE)
```

```python
import jax
import jax.numpy as jnp
from jax import lax
from jax.sharding import Mesh
from jax.sharding import PartitionSpec as P

GROUP = 256
SEGMENT = 16


EPS = 1e-05
SEQ = ("row", "seg")


def shifted(block, axis, distance):
    devices = range(lax.axis_size(axis))
    route = [(i - distance, i) for i in devices if i - distance in devices]
    return lax.ppermute(block, axis, route)


def body(x_raw, bc_raw, gate_z, step_size, log_decay, doc_ids, conv_x, conv_bc, skip, norm_gain):
    rows_dev, head_cols = x_raw.shape
    heads_dev = step_size.shape[1]
    head_size = head_cols // heads_dev
    states = bc_raw.shape[1] // 2
    taps = conv_x.shape[0]
    seg = lax.axis_size("seg")
    per_owner = heads_dev // seg
    raw_all = jnp.concatenate([x_raw, bc_raw], axis=1)
    labels = doc_ids + 1
    edge = jnp.concatenate(
        [raw_all[rows_dev - (taps - 1) :], labels[rows_dev - (taps - 1) :, None].astype(jnp.bfloat16)], axis=1
    )
    edge = shifted(edge, SEQ, 1)
    edge_rows = edge[:, : raw_all.shape[1]]
    edge_docs = edge[:, raw_all.shape[1]].astype(jnp.int32)
    extended = jnp.concatenate([edge_rows, raw_all], axis=0)
    ext_docs = jnp.concatenate([edge_docs, labels], axis=0)
    kernel = jnp.concatenate([conv_x, conv_bc], axis=1)
    total = jnp.zeros(raw_all.shape, jnp.float32)
    for k in range(taps):
        moved = extended[taps - 1 - k : taps - 1 - k + rows_dev].astype(jnp.float32)
        keep = (ext_docs[taps - 1 - k : taps - 1 - k + rows_dev] == labels).astype(jnp.float32)
        total = total + kernel[k][None, :] * moved * keep[:, None]
    activated = jax.nn.silu(total).astype(jnp.bfloat16)
    xconv = activated[:, :head_cols].reshape(rows_dev, heads_dev, head_size)
    bconv = activated[:, head_cols : head_cols + states]
    cconv = activated[:, head_cols + states :]
    xdt = (xconv.astype(jnp.float32) * step_size[:, :, None]).astype(jnp.bfloat16)
    lower = jnp.arange(GROUP)[:, None] >= jnp.arange(GROUP)[None, :]
    previous = edge_docs[taps - 2] - 1
    cum = jnp.cumsum(log_decay, axis=0)
    gram = jnp.dot(cconv, bconv.T, preferred_element_type=jnp.float32)
    mask = ((doc_ids[:, None] == doc_ids[None, :]) & lower)[None]
    diff = cum.T[:, :, None] - cum.T[:, None, :]
    weights = (jnp.where(mask, jnp.exp(jnp.where(mask, diff, 0.0)), 0.0) * gram[None]).astype(
        jnp.bfloat16
    )
    inners = jnp.einsum("hts,shp->thp", weights, xdt, preferred_element_type=jnp.float32)
    cont = (doc_ids == previous).astype(jnp.float32)
    entries = jnp.exp(cum) * cont[:, None]
    ends = jnp.where((doc_ids == doc_ids[-1])[:, None], jnp.exp(cum[-1][None, :] - cum), 0.0)
    written = (xdt.astype(jnp.float32) * ends[:, :, None]).astype(jnp.bfloat16)
    local = jnp.einsum("shp,sn->hpn", written, bconv, preferred_element_type=jnp.float32)
    through = jnp.exp(cum[-1]) * cont[-1]

    flat = head_size * states
    payload = jnp.concatenate(
        [local.reshape(heads_dev, flat), jnp.broadcast_to(through[:, None], (heads_dev, 128))], axis=1
    )
    got = lax.all_to_all(payload, "seg", 0, 0, tiled=True).reshape(seg, per_owner, flat + 128)
    pieces = got[:, :, :flat].reshape(seg, per_owner, head_size, states)
    decays = got[:, :, flat]
    folds = []
    decay_before = []
    running = jnp.zeros((per_owner, head_size, states), jnp.float32)
    product = jnp.ones((per_owner,), jnp.float32)
    for i in range(seg):
        folds.append(running)
        decay_before.append(product)
        running = decays[i][:, None, None] * running + pieces[i]
        product = product * decays[i]
    carry = shifted(running, "row", 1)
    entering = jnp.stack(decay_before)[:, :, None, None] * carry[None] + jnp.stack(folds)
    entered = lax.all_to_all(entering.astype(jnp.bfloat16), "seg", 0, 0, tiled=True).reshape(
        heads_dev, head_size, states
    )

    carried = (
        jnp.einsum("tn,hpn->thp", cconv, entered, preferred_element_type=jnp.float32)
        * entries[:, :, None]
    )
    scanned = inners + carried + skip[None, :, None] * xconv.astype(jnp.float32)
    gated_rows = scanned.reshape(GROUP, head_cols) * jax.nn.silu(gate_z.astype(jnp.float32))
    squares = lax.psum(jnp.sum(gated_rows * gated_rows, axis=1), "head")
    scale = lax.rsqrt(squares / (head_cols * lax.axis_size("head")) + EPS)
    return (gated_rows * scale[:, None] * norm_gain[None, :]).astype(jnp.bfloat16)


def solution(mesh):
    seq_size = mesh.shape["seq"]
    grid = Mesh(
        mesh.devices.reshape(seq_size // SEGMENT, SEGMENT, mesh.shape["head"]), ("row", "seg", "head")
    )
    return jax.shard_map(
        body,
        mesh=grid,
        in_specs=(
            P(SEQ, "head"),
            P(SEQ, None),
            P(SEQ, "head"),
            P(SEQ, "head"),
            P(SEQ, "head"),
            P(SEQ),
            P(None, "head"),
            P(),
            P("head"),
            P("head"),
        ),
        out_specs=P(SEQ, "head"),
        check_vma=False,
    )
```

```python
import jax
import jax.numpy as jnp
from jax import lax
from jax.sharding import Mesh
from jax.sharding import PartitionSpec as P

GROUP = 256
SEGMENT = 16


EPS = 1e-05
SEQ = ("row", "seg")


def shifted(block, axis, distance):
    devices = range(lax.axis_size(axis))
    route = [(i - distance, i) for i in devices if i - distance in devices]
    return lax.ppermute(block, axis, route)


def body(x_raw, bc_raw, gate_z, step_size, log_decay, doc_ids, conv_x, conv_bc, skip, norm_gain):
    rows_dev, head_cols = x_raw.shape
    heads_dev = step_size.shape[1]
    head_size = head_cols // heads_dev
    states = bc_raw.shape[1] // 2
    taps = conv_x.shape[0]
    seg = lax.axis_size("seg")
    per_owner = heads_dev // seg
    raw_all = jnp.concatenate([x_raw, bc_raw], axis=1)
    labels = doc_ids + 1
    edge = jnp.concatenate(
        [raw_all[rows_dev - (taps - 1) :], labels[rows_dev - (taps - 1) :, None].astype(jnp.bfloat16)], axis=1
    )
    edge = shifted(edge, SEQ, 1)
    edge_rows = edge[:, : raw_all.shape[1]]
    edge_docs = edge[:, raw_all.shape[1]].astype(jnp.int32)
    extended = jnp.concatenate([edge_rows, raw_all], axis=0)
    ext_docs = jnp.concatenate([edge_docs, labels], axis=0)
    kernel = jnp.concatenate([conv_x, conv_bc], axis=1)
    total = jnp.zeros(raw_all.shape, jnp.float32)
    for k in range(taps):
        moved = extended[taps - 1 - k : taps - 1 - k + rows_dev].astype(jnp.float32)
        keep = (ext_docs[taps - 1 - k : taps - 1 - k + rows_dev] == labels).astype(jnp.float32)
        total = total + kernel[k][None, :] * moved * keep[:, None]
    activated = jax.nn.silu(total).astype(jnp.bfloat16)
    xconv = activated[:, :head_cols].reshape(rows_dev, heads_dev, head_size)
    bconv = activated[:, head_cols : head_cols + states]
    cconv = activated[:, head_cols + states :]
    xdt = (xconv.astype(jnp.float32) * step_size[:, :, None]).astype(jnp.bfloat16)
    lower = jnp.arange(GROUP)[:, None] >= jnp.arange(GROUP)[None, :]
    previous = edge_docs[taps - 2] - 1
    cum = jnp.cumsum(log_decay, axis=0)
    gram = jnp.dot(cconv, bconv.T, preferred_element_type=jnp.float32)
    mask = ((doc_ids[:, None] == doc_ids[None, :]) & lower)[None]
    diff = cum.T[:, :, None] - cum.T[:, None, :]
    weights = (jnp.where(mask, jnp.exp(jnp.where(mask, diff, 0.0)), 0.0) * gram[None]).astype(
        jnp.bfloat16
    )
    inners = jnp.einsum("hts,shp->thp", weights, xdt, preferred_element_type=jnp.float32)
    cont = (doc_ids == previous).astype(jnp.float32)
    entries = jnp.exp(cum) * cont[:, None]
    ends = jnp.where((doc_ids == doc_ids[-1])[:, None], jnp.exp(cum[-1][None, :] - cum), 0.0)
    written = (xdt.astype(jnp.float32) * ends[:, :, None]).astype(jnp.bfloat16)
    local = jnp.einsum("shp,sn->hpn", written, bconv, preferred_element_type=jnp.float32)
    through = jnp.exp(cum[-1]) * cont[-1]

    flat = head_size * states
    payload = jnp.concatenate(
        [local.reshape(heads_dev, flat), jnp.broadcast_to(through[:, None], (heads_dev, 128))], axis=1
    )
    got = lax.all_to_all(payload, "seg", 0, 0, tiled=True).reshape(seg, per_owner, flat + 128)
    pieces = jnp.transpose(got[:, :, :flat], (1, 0, 2))
    decays = got[:, :, flat].T
    after = jnp.arange(seg + 1)[:, None, None]
    source = jnp.arange(seg)[None, :, None]
    between = (source < jnp.arange(seg)[None, None, :]) & (jnp.arange(seg)[None, None, :] < after)
    spans = jnp.prod(jnp.where(between[None], decays[:, None, None, :], 1.0), axis=3)
    weights_to = jnp.where((source[..., 0] < after[..., 0])[None], spans, 0.0)
    head_first = jnp.prod(
        jnp.where(jnp.arange(seg)[None, :] < jnp.arange(seg)[:, None], decays[:, None, :], 1.0), axis=2
    )
    exact = lax.Precision.HIGHEST
    total_row = jnp.einsum("gj,gjf->gf", weights_to[:, seg], pieces, precision=exact)
    carry = shifted(total_row, "row", 1)
    folds = jnp.einsum("gij,gjf->gif", weights_to[:, :seg], pieces, precision=exact)
    entering = head_first[:, :, None] * carry[:, None, :] + folds
    entering = jnp.transpose(entering, (1, 0, 2)).reshape(seg, per_owner, head_size, states)
    entered = lax.all_to_all(entering.astype(jnp.bfloat16), "seg", 0, 0, tiled=True).reshape(
        heads_dev, head_size, states
    )

    carried = (
        jnp.einsum("tn,hpn->thp", cconv, entered, preferred_element_type=jnp.float32)
        * entries[:, :, None]
    )
    scanned = inners + carried + skip[None, :, None] * xconv.astype(jnp.float32)
    gated_rows = scanned.reshape(GROUP, head_cols) * jax.nn.silu(gate_z.astype(jnp.float32))
    own = jnp.sum(gated_rows * gated_rows, axis=1)
    width = lax.axis_size("head")
    me = lax.axis_index("head")
    parts = [own] + [
        lax.ppermute(own, "head", [(i, (i + d) % width) for i in range(width)]) for d in range(1, width)
    ]
    squares = sum(
        sum(jnp.where((me - d) % width == src, parts[d], 0.0) for d in range(width)) for src in range(width)
    )
    scale = lax.rsqrt(squares / (head_cols * lax.axis_size("head")) + EPS)
    return (gated_rows * scale[:, None] * norm_gain[None, :]).astype(jnp.bfloat16)


def solution(mesh):
    seq_size = mesh.shape["seq"]
    grid = Mesh(
        mesh.devices.reshape(seq_size // SEGMENT, SEGMENT, mesh.shape["head"]), ("row", "seg", "head")
    )
    return jax.shard_map(
        body,
        mesh=grid,
        in_specs=(
            P(SEQ, "head"),
            P(SEQ, None),
            P(SEQ, "head"),
            P(SEQ, "head"),
            P(SEQ, "head"),
            P(SEQ),
            P(None, "head"),
            P(),
            P("head"),
            P("head"),
        ),
        out_specs=P(SEQ, "head"),
        check_vma=False,
    )
```

```python
import jax
import jax.numpy as jnp
from jax import lax
from jax.sharding import Mesh
from jax.sharding import PartitionSpec as P

GROUP = 256
SEGMENT = 16


EPS = 1e-05
SEQ = ("row", "seg")


def shifted(block, axis, distance):
    devices = range(lax.axis_size(axis))
    route = [(i - distance, i) for i in devices if i - distance in devices]
    return lax.ppermute(block, axis, route)


def body(x_raw, bc_raw, gate_z, step_size, log_decay, doc_ids, conv_x, conv_bc, skip, norm_gain):
    rows_dev, head_cols = x_raw.shape
    heads_dev = step_size.shape[1]
    head_size = head_cols // heads_dev
    states = bc_raw.shape[1] // 2
    taps = conv_x.shape[0]
    raw_all = jnp.concatenate([x_raw, bc_raw], axis=1)
    labels = doc_ids + 1
    edge = jnp.concatenate(
        [raw_all[rows_dev - (taps - 1) :], labels[rows_dev - (taps - 1) :, None].astype(jnp.bfloat16)], axis=1
    )
    edge = shifted(edge, SEQ, 1)
    edge_rows = edge[:, : raw_all.shape[1]]
    edge_docs = edge[:, raw_all.shape[1]].astype(jnp.int32)
    extended = jnp.concatenate([edge_rows, raw_all], axis=0)
    ext_docs = jnp.concatenate([edge_docs, labels], axis=0)
    kernel = jnp.concatenate([conv_x, conv_bc], axis=1)
    total = jnp.zeros(raw_all.shape, jnp.float32)
    for k in range(taps):
        moved = extended[taps - 1 - k : taps - 1 - k + rows_dev].astype(jnp.float32)
        keep = (ext_docs[taps - 1 - k : taps - 1 - k + rows_dev] == labels).astype(jnp.float32)
        total = total + kernel[k][None, :] * moved * keep[:, None]
    activated = jax.nn.silu(total).astype(jnp.bfloat16)
    xconv = activated[:, :head_cols].reshape(rows_dev, heads_dev, head_size)
    bconv = activated[:, head_cols : head_cols + states]
    cconv = activated[:, head_cols + states :]
    xdt = (xconv.astype(jnp.float32) * step_size[:, :, None]).astype(jnp.bfloat16)
    lower = jnp.arange(GROUP)[:, None] >= jnp.arange(GROUP)[None, :]
    previous = edge_docs[taps - 2] - 1
    cum = jnp.cumsum(log_decay, axis=0)
    gram = jnp.dot(cconv, bconv.T, preferred_element_type=jnp.float32)
    mask = ((doc_ids[:, None] == doc_ids[None, :]) & lower)[None]
    diff = cum.T[:, :, None] - cum.T[:, None, :]
    weights = (jnp.where(mask, jnp.exp(jnp.where(mask, diff, 0.0)), 0.0) * gram[None]).astype(
        jnp.bfloat16
    )
    inners = jnp.einsum("hts,shp->thp", weights, xdt, preferred_element_type=jnp.float32)
    cont = (doc_ids == previous).astype(jnp.float32)
    entries = jnp.exp(cum) * cont[:, None]
    ends = jnp.where((doc_ids == doc_ids[-1])[:, None], jnp.exp(cum[-1][None, :] - cum), 0.0)
    written = (xdt.astype(jnp.float32) * ends[:, :, None]).astype(jnp.bfloat16)
    local = jnp.einsum("shp,sn->hpn", written, bconv, preferred_element_type=jnp.float32)
    through = jnp.exp(cum[-1]) * cont[-1]

    owners = lax.axis_size(SEQ)
    rows_per = heads_dev * head_size // owners
    width = rows_per * states
    payload = jnp.concatenate(
        [
            local.reshape(owners, width),
            jnp.broadcast_to(jnp.repeat(through, owners // heads_dev)[:, None], (owners, 128)),
        ],
        axis=1,
    )
    got = lax.all_to_all(payload, SEQ, 0, 0, tiled=True)
    pieces = got[:, :width]
    decays = got[:, width]
    after = jnp.arange(owners)[:, None, None]
    source = jnp.arange(owners)[None, :, None]
    middle = jnp.arange(owners)[None, None, :]
    between = (source < middle) & (middle < after)
    spans = jnp.prod(jnp.where(between, decays[None, None, :], 1.0), axis=2)
    weights_to = jnp.where(source[..., 0] < after[..., 0], spans, 0.0)
    entering = jnp.dot(weights_to, pieces, precision=lax.Precision.HIGHEST)
    entered = lax.all_to_all(entering.astype(jnp.bfloat16), SEQ, 0, 0, tiled=True).reshape(
        heads_dev, head_size, states
    )

    carried = (
        jnp.einsum("tn,hpn->thp", cconv, entered, preferred_element_type=jnp.float32)
        * entries[:, :, None]
    )
    scanned = inners + carried + skip[None, :, None] * xconv.astype(jnp.float32)
    gated_rows = scanned.reshape(GROUP, head_cols) * jax.nn.silu(gate_z.astype(jnp.float32))
    own = jnp.sum(gated_rows * gated_rows, axis=1)
    ways = lax.axis_size("head")
    each = lax.all_to_all(jnp.broadcast_to(own[None], (ways, own.shape[0])), "head", 0, 0, tiled=True)
    squares = each[0]
    for src in range(1, ways):
        squares = squares + each[src]
    scale = lax.rsqrt(squares / (head_cols * lax.axis_size("head")) + EPS)
    return (gated_rows * scale[:, None] * norm_gain[None, :]).astype(jnp.bfloat16)


def solution(mesh):
    seq_size = mesh.shape["seq"]
    grid = Mesh(
        mesh.devices.reshape(seq_size // SEGMENT, SEGMENT, mesh.shape["head"]), ("row", "seg", "head")
    )
    return jax.shard_map(
        body,
        mesh=grid,
        in_specs=(
            P(SEQ, "head"),
            P(SEQ, None),
            P(SEQ, "head"),
            P(SEQ, "head"),
            P(SEQ, "head"),
            P(SEQ),
            P(None, "head"),
            P(),
            P("head"),
            P("head"),
        ),
        out_specs=P(SEQ, "head"),
        check_vma=False,
    )
```

```python
import jax
import jax.numpy as jnp
from jax import lax
from jax.sharding import Mesh
from jax.sharding import PartitionSpec as P

GROUP = 256
SEGMENT = 16


EPS = 1e-05
SEQ = ("row", "seg")


def shifted(block, axis, distance):
    devices = range(lax.axis_size(axis))
    route = [(i - distance, i) for i in devices if i - distance in devices]
    return lax.ppermute(block, axis, route)


def body(x_raw, bc_raw, gate_z, step_size, log_decay, doc_ids, conv_x, conv_bc, skip, norm_gain):
    rows_dev, head_cols = x_raw.shape
    heads_dev = step_size.shape[1]
    head_size = head_cols // heads_dev
    states = bc_raw.shape[1] // 2
    taps = conv_x.shape[0]
    seg = lax.axis_size("seg")
    per_owner = heads_dev // seg
    raw_all = jnp.concatenate([x_raw, bc_raw], axis=1)
    labels = doc_ids + 1
    edge = jnp.concatenate(
        [raw_all[rows_dev - (taps - 1) :], labels[rows_dev - (taps - 1) :, None].astype(jnp.bfloat16)], axis=1
    )
    edge = shifted(edge, SEQ, 1)
    edge_rows = edge[:, : raw_all.shape[1]]
    edge_docs = edge[:, raw_all.shape[1]].astype(jnp.int32)
    extended = jnp.concatenate([edge_rows, raw_all], axis=0)
    ext_docs = jnp.concatenate([edge_docs, labels], axis=0)
    kernel = jnp.concatenate([conv_x, conv_bc], axis=1)
    total = jnp.zeros(raw_all.shape, jnp.float32)
    for k in range(taps):
        moved = extended[taps - 1 - k : taps - 1 - k + rows_dev].astype(jnp.float32)
        keep = (ext_docs[taps - 1 - k : taps - 1 - k + rows_dev] == labels).astype(jnp.float32)
        total = total + kernel[k][None, :] * moved * keep[:, None]
    activated = jax.nn.silu(total).astype(jnp.bfloat16)
    xconv = activated[:, :head_cols].reshape(rows_dev, heads_dev, head_size)
    bconv = activated[:, head_cols : head_cols + states]
    cconv = activated[:, head_cols + states :]
    xdt = (xconv.astype(jnp.float32) * step_size[:, :, None]).astype(jnp.bfloat16)
    lower = jnp.arange(GROUP)[:, None] >= jnp.arange(GROUP)[None, :]
    previous = edge_docs[taps - 2] - 1
    cum = jnp.cumsum(log_decay, axis=0)
    gram = jnp.dot(cconv, bconv.T, preferred_element_type=jnp.float32)
    mask = ((doc_ids[:, None] == doc_ids[None, :]) & lower)[None]
    diff = cum.T[:, :, None] - cum.T[:, None, :]
    weights = (jnp.where(mask, jnp.exp(jnp.where(mask, diff, 0.0)), 0.0) * gram[None]).astype(
        jnp.bfloat16
    )
    inners = jnp.einsum("hts,shp->thp", weights, xdt, preferred_element_type=jnp.float32)
    cont = (doc_ids == previous).astype(jnp.float32)
    entries = jnp.exp(cum) * cont[:, None]
    ends = jnp.where((doc_ids == doc_ids[-1])[:, None], jnp.exp(cum[-1][None, :] - cum), 0.0)
    written = (xdt.astype(jnp.float32) * ends[:, :, None]).astype(jnp.bfloat16)
    local = jnp.einsum("shp,sn->hpn", written, bconv, preferred_element_type=jnp.float32)
    through = jnp.exp(cum[-1]) * cont[-1]

    flat = head_size * states
    payload = jnp.concatenate(
        [local.reshape(heads_dev, flat), jnp.broadcast_to(through[:, None], (heads_dev, 128))], axis=1
    )
    got = lax.all_to_all(payload, "seg", 0, 0, tiled=True).reshape(seg, per_owner, flat + 128)
    pieces = jnp.transpose(got[:, :, :flat], (1, 0, 2))
    decays = got[:, :, flat].T
    after = jnp.arange(seg + 1)[:, None, None]
    source = jnp.arange(seg)[None, :, None]
    between = (source < jnp.arange(seg)[None, None, :]) & (jnp.arange(seg)[None, None, :] < after)
    spans = jnp.prod(jnp.where(between[None], decays[:, None, None, :], 1.0), axis=3)
    weights_to = jnp.where((source[..., 0] < after[..., 0])[None], spans, 0.0)
    head_first = jnp.prod(
        jnp.where(jnp.arange(seg)[None, :] < jnp.arange(seg)[:, None], decays[:, None, :], 1.0), axis=2
    )
    exact = lax.Precision.HIGHEST
    total_row = jnp.einsum("gj,gjf->gf", weights_to[:, seg], pieces, precision=exact)
    carry = shifted(total_row, "row", 1)
    folds = jnp.einsum("gij,gjf->gif", weights_to[:, :seg], pieces, precision=exact)
    entering = head_first[:, :, None] * carry[:, None, :] + folds
    entering = jnp.transpose(entering, (1, 0, 2)).reshape(seg, per_owner, head_size, states)
    entered = lax.all_to_all(entering.astype(jnp.bfloat16), "seg", 0, 0, tiled=True).reshape(
        heads_dev, head_size, states
    )

    carried = (
        jnp.einsum("tn,hpn->thp", cconv, entered, preferred_element_type=jnp.float32)
        * entries[:, :, None]
    )
    scanned = inners + carried + skip[None, :, None] * xconv.astype(jnp.float32)
    gated_rows = scanned.reshape(GROUP, head_cols) * jax.nn.silu(gate_z.astype(jnp.float32))
    own = jnp.sum(gated_rows * gated_rows, axis=1)
    ways = lax.axis_size("head")
    each = lax.all_to_all(jnp.broadcast_to(own[None], (ways, own.shape[0])), "head", 0, 0, tiled=True)
    squares = each[0]
    for src in range(1, ways):
        squares = squares + each[src]
    scale = lax.rsqrt(squares / (head_cols * lax.axis_size("head")) + EPS)
    return (gated_rows * scale[:, None] * norm_gain[None, :]).astype(jnp.bfloat16)


def solution(mesh):
    seq_size = mesh.shape["seq"]
    grid = Mesh(
        mesh.devices.reshape(seq_size // SEGMENT, SEGMENT, mesh.shape["head"]), ("row", "seg", "head")
    )
    return jax.shard_map(
        body,
        mesh=grid,
        in_specs=(
            P(SEQ, "head"),
            P(SEQ, None),
            P(SEQ, "head"),
            P(SEQ, "head"),
            P(SEQ, "head"),
            P(SEQ),
            P(None, "head"),
            P(),
            P("head"),
            P("head"),
        ),
        out_specs=P(SEQ, "head"),
        check_vma=False,
    )
```

```python
import jax
import jax.numpy as jnp
from jax import lax
from jax.sharding import Mesh
from jax.sharding import PartitionSpec as P

GROUP = 256
SEGMENT = 16


EPS = 1e-05
SEQ = ("row", "seg")


def shifted(block, axis, distance):
    devices = range(lax.axis_size(axis))
    route = [(i - distance, i) for i in devices if i - distance in devices]
    return lax.ppermute(block, axis, route)


def body(x_raw, bc_raw, gate_z, step_size, log_decay, doc_ids, conv_x, conv_bc, skip, norm_gain):
    rows_dev, head_cols = x_raw.shape
    heads_dev = step_size.shape[1]
    head_size = head_cols // heads_dev
    states = bc_raw.shape[1] // 2
    taps = conv_x.shape[0]
    seg = lax.axis_size("seg")
    halo = taps - 1
    edge = jnp.concatenate(
        [x_raw[rows_dev - halo :], bc_raw[rows_dev - halo :], doc_ids[rows_dev - halo :, None].astype(jnp.bfloat16)],
        axis=1,
    )
    edge = shifted(edge, SEQ, 1)
    edge_docs = edge[:, head_cols + 2 * states].astype(jnp.int32)
    ext_docs = jnp.concatenate([edge_docs, doc_ids], axis=0)
    keeps = [(ext_docs[halo - k : halo - k + rows_dev] == doc_ids).astype(jnp.float32) for k in range(taps)]

    def conv(raw, edge_rows, taps_w):
        extended = jnp.concatenate([edge_rows, raw], axis=0)
        total = jnp.zeros(raw.shape, jnp.float32)
        for k in range(taps):
            moved = extended[halo - k : halo - k + rows_dev].astype(jnp.float32)
            total = total + taps_w[k][None, :] * moved * keeps[k][:, None]
        return jax.nn.silu(total).astype(jnp.bfloat16)

    xflat = conv(x_raw, edge[:, :head_cols], conv_x)
    bcconv = conv(bc_raw, edge[:, head_cols : head_cols + 2 * states], conv_bc)
    xconv = xflat.reshape(rows_dev, heads_dev, head_size)
    bconv = bcconv[:, :states]
    cconv = bcconv[:, states:]
    xdt = (xconv.astype(jnp.float32) * step_size[:, :, None]).astype(jnp.bfloat16)
    lower = jnp.arange(GROUP)[:, None] >= jnp.arange(GROUP)[None, :]
    previous = edge_docs[halo - 1]
    cum = jnp.cumsum(log_decay, axis=0)
    gram = jnp.dot(cconv, bconv.T, preferred_element_type=jnp.float32)
    mask = ((doc_ids[:, None] == doc_ids[None, :]) & lower)[None]
    diff = cum.T[:, :, None] - cum.T[:, None, :]
    weights = (jnp.where(mask, jnp.exp(jnp.where(mask, diff, 0.0)), 0.0) * gram[None]).astype(
        jnp.bfloat16
    )
    inners = jnp.einsum("hts,shp->thp", weights, xdt, preferred_element_type=jnp.float32)
    cont = (doc_ids == previous).astype(jnp.float32)
    entries = jnp.exp(cum) * cont[:, None]
    ends = jnp.where((doc_ids == doc_ids[-1])[:, None], jnp.exp(cum[-1][None, :] - cum), 0.0)
    written = (xdt.astype(jnp.float32) * ends[:, :, None]).astype(jnp.bfloat16)
    local = jnp.einsum("shp,sn->hpn", written, bconv, preferred_element_type=jnp.float32)
    through = jnp.exp(cum[-1]) * cont[-1]

    flat = head_size * states
    payload = jnp.concatenate(
        [local.reshape(heads_dev, flat), jnp.broadcast_to(through[:, None], (heads_dev, 128))], axis=1
    )
    got = lax.all_to_all(payload, "seg", 0, 0, tiled=True)
    pieces = got[:, :flat]
    decays = got[:, flat]
    after = jnp.arange(seg + 1)[:, None, None]
    source = jnp.arange(seg)[None, :, None]
    middle = jnp.arange(seg)[None, None, :]
    spans = jnp.prod(jnp.where((source < middle) & (middle < after), decays[None, None, :], 1.0), axis=2)
    weights_to = jnp.where(source[..., 0] < after[..., 0], spans, 0.0)
    exact = lax.Precision.HIGHEST
    carry = shifted(jnp.dot(weights_to[seg], pieces, precision=exact), "row", 1)
    head_first = jnp.prod(jnp.where(middle[0] < after[:seg, :, 0], decays[None, :], 1.0), axis=1)
    entering = head_first[:, None] * carry[None, :] + jnp.dot(weights_to[:seg], pieces, precision=exact)
    entered = lax.all_to_all(
        entering.astype(jnp.bfloat16).reshape(seg, head_size, states), "seg", 0, 0, tiled=True
    )

    carried = (
        jnp.einsum("tn,hpn->thp", cconv, entered, preferred_element_type=jnp.float32)
        * entries[:, :, None]
    )
    scanned = inners + carried + skip[None, :, None] * xconv.astype(jnp.float32)
    gated_rows = scanned.reshape(GROUP, head_cols) * jax.nn.silu(gate_z.astype(jnp.float32))
    own = jnp.sum(gated_rows * gated_rows, axis=1)
    ways = lax.axis_size("head")
    each = lax.all_to_all(jnp.broadcast_to(own[None], (ways, own.shape[0])), "head", 0, 0, tiled=True)
    squares = each[0]
    for src in range(1, ways):
        squares = squares + each[src]
    scale = lax.rsqrt(squares / (head_cols * lax.axis_size("head")) + EPS)
    return (gated_rows * scale[:, None] * norm_gain[None, :]).astype(jnp.bfloat16)


def solution(mesh):
    seq_size = mesh.shape["seq"]
    grid = Mesh(
        mesh.devices.reshape(seq_size // SEGMENT, SEGMENT, mesh.shape["head"]), ("row", "seg", "head")
    )
    return jax.shard_map(
        body,
        mesh=grid,
        in_specs=(
            P(SEQ, "head"),
            P(SEQ, None),
            P(SEQ, "head"),
            P(SEQ, "head"),
            P(SEQ, "head"),
            P(SEQ),
            P(None, "head"),
            P(),
            P("head"),
            P("head"),
        ),
        out_specs=P(SEQ, "head"),
        check_vma=False,
    )
```

```python
import jax
import jax.numpy as jnp
from jax import lax
from jax.sharding import Mesh
from jax.sharding import PartitionSpec as P

GROUP = 256
SEGMENT = 16


EPS = 1e-05
SEQ = ("row", "seg")


def shifted(block, axis, distance):
    devices = range(lax.axis_size(axis))
    route = [(i - distance, i) for i in devices if i - distance in devices]
    return lax.ppermute(block, axis, route)


def body(x_raw, bc_raw, gate_z, step_size, log_decay, doc_ids, conv_x, conv_bc, skip, norm_gain):
    rows_dev, head_cols = x_raw.shape
    heads_dev = step_size.shape[1]
    head_size = head_cols // heads_dev
    states = bc_raw.shape[1] // 2
    taps = conv_x.shape[0]
    seg = lax.axis_size("seg")
    per_owner = heads_dev // seg
    raw_all = jnp.concatenate([x_raw, bc_raw], axis=1)
    labels = doc_ids + 1
    edge = jnp.concatenate(
        [raw_all[rows_dev - (taps - 1) :], labels[rows_dev - (taps - 1) :, None].astype(jnp.bfloat16)], axis=1
    )
    edge = shifted(edge, SEQ, 1)
    edge_rows = edge[:, : raw_all.shape[1]]
    edge_docs = edge[:, raw_all.shape[1]].astype(jnp.int32)
    extended = jnp.concatenate([edge_rows, raw_all], axis=0)
    ext_docs = jnp.concatenate([edge_docs, labels], axis=0)
    kernel = jnp.concatenate([conv_x, conv_bc], axis=1)
    total = jnp.zeros(raw_all.shape, jnp.float32)
    for k in range(taps):
        moved = extended[taps - 1 - k : taps - 1 - k + rows_dev].astype(jnp.float32)
        keep = (ext_docs[taps - 1 - k : taps - 1 - k + rows_dev] == labels).astype(jnp.float32)
        total = total + kernel[k][None, :] * moved * keep[:, None]
    activated = jax.nn.silu(total).astype(jnp.bfloat16)
    xconv = activated[:, :head_cols].reshape(rows_dev, heads_dev, head_size)
    bconv = activated[:, head_cols : head_cols + states]
    cconv = activated[:, head_cols + states :]
    xdt = (xconv.astype(jnp.float32) * step_size[:, :, None]).astype(jnp.bfloat16)
    lower = jnp.arange(GROUP)[:, None] >= jnp.arange(GROUP)[None, :]
    previous = edge_docs[taps - 2] - 1
    cum = jnp.cumsum(log_decay, axis=0)
    gram = jnp.dot(cconv, bconv.T, preferred_element_type=jnp.float32)
    mask = ((doc_ids[:, None] == doc_ids[None, :]) & lower)[None]
    diff = cum.T[:, :, None] - cum.T[:, None, :]
    weights = (jnp.where(mask, jnp.exp(jnp.where(mask, diff, 0.0)), 0.0) * gram[None]).astype(
        jnp.bfloat16
    )
    inners = jnp.einsum("hts,shp->thp", weights, xdt, preferred_element_type=jnp.float32)
    cont = (doc_ids == previous).astype(jnp.float32)
    entries = jnp.exp(cum) * cont[:, None]
    ends = jnp.where((doc_ids == doc_ids[-1])[:, None], jnp.exp(cum[-1][None, :] - cum), 0.0)
    written = (xdt.astype(jnp.float32) * ends[:, :, None]).astype(jnp.bfloat16)
    local = jnp.einsum("shp,sn->hpn", written, bconv, preferred_element_type=jnp.float32)
    through = jnp.exp(cum[-1]) * cont[-1]

    flat = head_size * states
    payload = jnp.concatenate(
        [local.reshape(heads_dev, flat), jnp.broadcast_to(through[:, None], (heads_dev, 128))], axis=1
    )
    got = lax.all_to_all(payload, "seg", 0, 0, tiled=True).reshape(seg, per_owner, flat + 128)
    pieces = jnp.transpose(got[:, :, :flat], (1, 0, 2))
    decays = got[:, :, flat].T
    after = jnp.arange(seg + 1)[:, None, None]
    source = jnp.arange(seg)[None, :, None]
    between = (source < jnp.arange(seg)[None, None, :]) & (jnp.arange(seg)[None, None, :] < after)
    spans = jnp.prod(jnp.where(between[None], decays[:, None, None, :], 1.0), axis=3)
    weights_to = jnp.where((source[..., 0] < after[..., 0])[None], spans, 0.0)
    head_first = jnp.prod(
        jnp.where(jnp.arange(seg)[None, :] < jnp.arange(seg)[:, None], decays[:, None, :], 1.0), axis=2
    )
    exact = lax.Precision.HIGHEST
    total_row = jnp.einsum("gj,gjf->gf", weights_to[:, seg], pieces, precision=exact)
    carry = shifted(total_row, "row", 1)
    folds = jnp.einsum("gij,gjf->gif", weights_to[:, :seg], pieces, precision=exact)
    entering = head_first[:, :, None] * carry[:, None, :] + folds
    entering = jnp.transpose(entering, (1, 0, 2)).reshape(seg, per_owner, head_size, states)
    entered = lax.all_to_all(entering.astype(jnp.bfloat16), "seg", 0, 0, tiled=True).reshape(
        heads_dev, head_size, states
    )

    carried = (
        jnp.einsum("tn,hpn->thp", cconv, entered, preferred_element_type=jnp.float32)
        * entries[:, :, None]
    )
    skipped, gate = lax.optimization_barrier(
        (skip[None, :, None] * xconv.astype(jnp.float32), jax.nn.silu(gate_z.astype(jnp.float32)))
    )
    scanned = inners + carried + skipped
    gated_rows = scanned.reshape(GROUP, head_cols) * gate
    own = jnp.sum(gated_rows * gated_rows, axis=1)
    ways = lax.axis_size("head")
    each = lax.all_to_all(jnp.broadcast_to(own[None], (ways, own.shape[0])), "head", 0, 0, tiled=True)
    squares = each[0]
    for src in range(1, ways):
        squares = squares + each[src]
    scale = lax.rsqrt(squares / (head_cols * lax.axis_size("head")) + EPS)
    return (gated_rows * scale[:, None] * norm_gain[None, :]).astype(jnp.bfloat16)


def solution(mesh):
    seq_size = mesh.shape["seq"]
    grid = Mesh(
        mesh.devices.reshape(seq_size // SEGMENT, SEGMENT, mesh.shape["head"]), ("row", "seg", "head")
    )
    return jax.shard_map(
        body,
        mesh=grid,
        in_specs=(
            P(SEQ, "head"),
            P(SEQ, None),
            P(SEQ, "head"),
            P(SEQ, "head"),
            P(SEQ, "head"),
            P(SEQ),
            P(None, "head"),
            P(),
            P("head"),
            P("head"),
        ),
        out_specs=P(SEQ, "head"),
        check_vma=False,
    )
```

```python
import jax
import jax.numpy as jnp
from jax import lax
from jax.experimental import pallas as pl
from jax.experimental.pallas import tpu as pltpu
from jax.sharding import Mesh
from jax.sharding import PartitionSpec as P

GROUP = 256
SEGMENT = 16


EPS = 1e-05
SEQ = ("row", "seg")


def shifted(block, axis, distance):
    devices = range(lax.axis_size(axis))
    route = [(i - distance, i) for i in devices if i - distance in devices]
    return lax.ppermute(block, axis, route)


def front_kernel(x_ref, bc_ref, edge_ref, keep_ref, cx_ref, cb_ref, step_ref, ends_ref,
                 actx_ref, actbc_ref, xdt_ref, local_ref, extx, extb):
    rows, head_cols = x_ref.shape
    both = bc_ref.shape[1]
    pad = edge_ref.shape[0]
    extx[0:pad, :] = edge_ref[:, 0:head_cols].astype(jnp.float32)
    extx[pad : pad + rows, :] = x_ref[...].astype(jnp.float32)
    extb[0:pad, :] = edge_ref[:, head_cols : head_cols + both].astype(jnp.float32)
    extb[pad : pad + rows, :] = bc_ref[...].astype(jnp.float32)

    def conv(ext, w_ref):
        total = jnp.zeros((rows, ext.shape[1]), jnp.float32)
        for k in range(w_ref.shape[0]):
            moved = ext[pl.ds(pad - k, rows), :]
            total = total + w_ref[k : k + 1, :] * moved * keep_ref[:, k : k + 1]
        return jax.nn.silu(total).astype(jnp.bfloat16)

    ax = conv(extx, cx_ref)
    ab = conv(extb, cb_ref)
    actx_ref[...] = ax
    actbc_ref[...] = ab
    xdt = (ax.astype(jnp.float32) * step_ref[...]).astype(jnp.bfloat16)
    xdt_ref[...] = xdt
    written = (xdt.astype(jnp.float32) * ends_ref[...]).astype(jnp.bfloat16)
    states = local_ref.shape[1]
    local_ref[...] = lax.dot_general(
        written, ab[:, 0:states], (((0,), (0,)), ((), ())), preferred_element_type=jnp.float32
    )


def front(x_raw, bc_raw, edge, keeps, conv_x, conv_bc, step_e, ends_e):
    rows, head_cols = x_raw.shape
    both = bc_raw.shape[1]
    vmem = pl.BlockSpec(memory_space=pltpu.VMEM)
    return pl.pallas_call(
        front_kernel,
        out_shape=(
            jax.ShapeDtypeStruct((rows, head_cols), jnp.bfloat16),
            jax.ShapeDtypeStruct((rows, both), jnp.bfloat16),
            jax.ShapeDtypeStruct((rows, head_cols), jnp.bfloat16),
            jax.ShapeDtypeStruct((head_cols, both // 2), jnp.float32),
        ),
        in_specs=[vmem] * 8,
        out_specs=(vmem, vmem, vmem, vmem),
        scratch_shapes=[
            pltpu.VMEM((rows + edge.shape[0], head_cols), jnp.float32),
            pltpu.VMEM((rows + edge.shape[0], both), jnp.float32),
        ],
    )(x_raw, bc_raw, edge, keeps, conv_x, conv_bc, step_e, ends_e)


def body(x_raw, bc_raw, gate_z, step_size, log_decay, doc_ids, conv_x, conv_bc, skip, norm_gain):
    rows_dev, head_cols = x_raw.shape
    heads_dev = step_size.shape[1]
    head_size = head_cols // heads_dev
    states = bc_raw.shape[1] // 2
    taps = conv_x.shape[0]
    seg = lax.axis_size("seg")
    per_owner = heads_dev // seg
    pad = 8
    labels = doc_ids + 1
    edge = jnp.concatenate(
        [x_raw[rows_dev - pad :], bc_raw[rows_dev - pad :], labels[rows_dev - pad :, None].astype(jnp.bfloat16)],
        axis=1,
    )
    edge = shifted(edge, SEQ, 1)
    edge_docs = edge[:, head_cols + 2 * states].astype(jnp.int32)
    ext_docs = jnp.concatenate([edge_docs, labels], axis=0)
    keeps = jnp.stack(
        [(ext_docs[pad - k : pad - k + rows_dev] == labels).astype(jnp.float32) for k in range(taps)], axis=1
    )
    previous = edge_docs[pad - 1] - 1
    cum = jnp.cumsum(log_decay, axis=0)
    ends = jnp.where((doc_ids == doc_ids[-1])[:, None], jnp.exp(cum[-1][None, :] - cum), 0.0)
    xflat, bcconv, xdt_flat, local_flat = front(
        x_raw,
        bc_raw,
        edge,
        keeps,
        conv_x,
        conv_bc,
        jnp.repeat(step_size, head_size, axis=1),
        jnp.repeat(ends, head_size, axis=1),
    )
    xconv = xflat.reshape(rows_dev, heads_dev, head_size)
    bconv = bcconv[:, :states]
    cconv = bcconv[:, states:]
    xdt = xdt_flat.reshape(rows_dev, heads_dev, head_size)
    lower = jnp.arange(GROUP)[:, None] >= jnp.arange(GROUP)[None, :]
    gram = jnp.dot(cconv, bconv.T, preferred_element_type=jnp.float32)
    mask = ((doc_ids[:, None] == doc_ids[None, :]) & lower)[None]
    diff = cum.T[:, :, None] - cum.T[:, None, :]
    weights = (jnp.where(mask, jnp.exp(jnp.where(mask, diff, 0.0)), 0.0) * gram[None]).astype(
        jnp.bfloat16
    )
    inners = jnp.einsum("hts,shp->thp", weights, xdt, preferred_element_type=jnp.float32)
    cont = (doc_ids == previous).astype(jnp.float32)
    entries = jnp.exp(cum) * cont[:, None]
    local = local_flat.reshape(heads_dev, head_size, states)
    through = jnp.exp(cum[-1]) * cont[-1]

    flat = head_size * states
    payload = jnp.concatenate(
        [local.reshape(heads_dev, flat), jnp.broadcast_to(through[:, None], (heads_dev, 128))], axis=1
    )
    got = lax.all_to_all(payload, "seg", 0, 0, tiled=True).reshape(seg, per_owner, flat + 128)
    pieces = jnp.transpose(got[:, :, :flat], (1, 0, 2))
    decays = got[:, :, flat].T
    after = jnp.arange(seg + 1)[:, None, None]
    source = jnp.arange(seg)[None, :, None]
    between = (source < jnp.arange(seg)[None, None, :]) & (jnp.arange(seg)[None, None, :] < after)
    spans = jnp.prod(jnp.where(between[None], decays[:, None, None, :], 1.0), axis=3)
    weights_to = jnp.where((source[..., 0] < after[..., 0])[None], spans, 0.0)
    head_first = jnp.prod(
        jnp.where(jnp.arange(seg)[None, :] < jnp.arange(seg)[:, None], decays[:, None, :], 1.0), axis=2
    )
    exact = lax.Precision.HIGHEST
    total_row = jnp.einsum("gj,gjf->gf", weights_to[:, seg], pieces, precision=exact)
    carry = shifted(total_row, "row", 1)
    folds = jnp.einsum("gij,gjf->gif", weights_to[:, :seg], pieces, precision=exact)
    entering = head_first[:, :, None] * carry[:, None, :] + folds
    entering = jnp.transpose(entering, (1, 0, 2)).reshape(seg, per_owner, head_size, states)
    entered = lax.all_to_all(entering.astype(jnp.bfloat16), "seg", 0, 0, tiled=True).reshape(
        heads_dev, head_size, states
    )

    carried = (
        jnp.einsum("tn,hpn->thp", cconv, entered, preferred_element_type=jnp.float32)
        * entries[:, :, None]
    )
    scanned = inners + carried + skip[None, :, None] * xconv.astype(jnp.float32)
    gated_rows = scanned.reshape(GROUP, head_cols) * jax.nn.silu(gate_z.astype(jnp.float32))
    own = jnp.sum(gated_rows * gated_rows, axis=1)
    ways = lax.axis_size("head")
    each = lax.all_to_all(jnp.broadcast_to(own[None], (ways, own.shape[0])), "head", 0, 0, tiled=True)
    squares = each[0]
    for src in range(1, ways):
        squares = squares + each[src]
    scale = lax.rsqrt(squares / (head_cols * lax.axis_size("head")) + EPS)
    return (gated_rows * scale[:, None] * norm_gain[None, :]).astype(jnp.bfloat16)


def solution(mesh):
    seq_size = mesh.shape["seq"]
    grid = Mesh(
        mesh.devices.reshape(seq_size // SEGMENT, SEGMENT, mesh.shape["head"]), ("row", "seg", "head")
    )
    return jax.shard_map(
        body,
        mesh=grid,
        in_specs=(
            P(SEQ, "head"),
            P(SEQ, None),
            P(SEQ, "head"),
            P(SEQ, "head"),
            P(SEQ, "head"),
            P(SEQ),
            P(None, "head"),
            P(),
            P("head"),
            P("head"),
        ),
        out_specs=P(SEQ, "head"),
        check_vma=False,
    )
```

```python
import jax
import jax.numpy as jnp
from jax import lax
from jax.sharding import Mesh
from jax.sharding import PartitionSpec as P

GROUP = 256
SEGMENT = 16


EPS = 1e-05
SEQ = ("row", "seg")


def shifted(block, axis, distance):
    devices = range(lax.axis_size(axis))
    route = [(i - distance, i) for i in devices if i - distance in devices]
    return lax.ppermute(block, axis, route)


def body(x_raw, bc_raw, gate_z, step_size, log_decay, doc_ids, conv_x, conv_bc, skip, norm_gain):
    rows_dev, head_cols = x_raw.shape
    heads_dev = step_size.shape[1]
    head_size = head_cols // heads_dev
    states = bc_raw.shape[1] // 2
    taps = conv_x.shape[0]
    seg = lax.axis_size("seg")
    raw_all = jnp.concatenate([x_raw, bc_raw], axis=1)
    labels = doc_ids + 1
    edge = jnp.concatenate(
        [raw_all[rows_dev - (taps - 1) :], labels[rows_dev - (taps - 1) :, None].astype(jnp.bfloat16)], axis=1
    )
    edge = shifted(edge, SEQ, 1)
    edge_rows = edge[:, : raw_all.shape[1]]
    edge_docs = edge[:, raw_all.shape[1]].astype(jnp.int32)
    extended = jnp.concatenate([edge_rows, raw_all], axis=0)
    ext_docs = jnp.concatenate([edge_docs, labels], axis=0)
    kernel = jnp.concatenate([conv_x, conv_bc], axis=1)
    total = jnp.zeros(raw_all.shape, jnp.float32)
    for k in range(taps):
        moved = extended[taps - 1 - k : taps - 1 - k + rows_dev].astype(jnp.float32)
        keep = (ext_docs[taps - 1 - k : taps - 1 - k + rows_dev] == labels).astype(jnp.float32)
        total = total + kernel[k][None, :] * moved * keep[:, None]
    activated = jax.nn.silu(total).astype(jnp.bfloat16)
    xconv = activated[:, :head_cols].reshape(rows_dev, heads_dev, head_size)
    bconv = activated[:, head_cols : head_cols + states]
    cconv = activated[:, head_cols + states :]
    xdt = (xconv.astype(jnp.float32) * step_size[:, :, None]).astype(jnp.bfloat16)
    lower = jnp.arange(GROUP)[:, None] >= jnp.arange(GROUP)[None, :]
    previous = edge_docs[taps - 2] - 1
    cum = jnp.cumsum(log_decay, axis=0)
    gram = jnp.dot(cconv, bconv.T, preferred_element_type=jnp.float32)
    mask = ((doc_ids[:, None] == doc_ids[None, :]) & lower)[None]
    diff = cum.T[:, :, None] - cum.T[:, None, :]
    weights = (jnp.where(mask, jnp.exp(jnp.where(mask, diff, 0.0)), 0.0) * gram[None]).astype(
        jnp.bfloat16
    )
    inners = jnp.einsum("hts,shp->thp", weights, xdt, preferred_element_type=jnp.float32)
    cont = (doc_ids == previous).astype(jnp.float32)
    entries = jnp.exp(cum) * cont[:, None]
    ends = jnp.where((doc_ids == doc_ids[-1])[:, None], jnp.exp(cum[-1][None, :] - cum), 0.0)
    written = (xdt.astype(jnp.float32) * ends[:, :, None]).astype(jnp.bfloat16)
    local = jnp.einsum("shp,sn->hpn", written, bconv, preferred_element_type=jnp.float32)
    through = jnp.exp(cum[-1]) * cont[-1]

    pad_rows = 8
    payload = jnp.concatenate(
        [local, jnp.broadcast_to(through[:, None, None], (heads_dev, pad_rows, states))], axis=1
    )
    got = lax.all_to_all(payload, "seg", 0, 0, tiled=True)
    pieces = got[:, :head_size, :]
    decays = got[:, head_size, 0]
    after = jnp.arange(seg + 1)[:, None, None]
    source = jnp.arange(seg)[None, :, None]
    middle = jnp.arange(seg)[None, None, :]
    spans = jnp.prod(jnp.where((source < middle) & (middle < after), decays[None, None, :], 1.0), axis=2)
    weights_to = jnp.where(source[..., 0] < after[..., 0], spans, 0.0)
    exact = lax.Precision.HIGHEST
    carry = shifted(jnp.einsum("j,jpn->pn", weights_to[seg], pieces, precision=exact), "row", 1)
    head_first = jnp.prod(jnp.where(middle[0] < after[:seg, :, 0], decays[None, :], 1.0), axis=1)
    folds = jnp.einsum("ij,jpn->ipn", weights_to[:seg], pieces, precision=exact)
    entering = head_first[:, None, None] * carry[None] + folds
    entered = lax.all_to_all(entering.astype(jnp.bfloat16), "seg", 0, 0, tiled=True)

    carried = (
        jnp.einsum("tn,hpn->thp", cconv, entered, preferred_element_type=jnp.float32)
        * entries[:, :, None]
    )
    scanned = inners + carried + skip[None, :, None] * xconv.astype(jnp.float32)
    gated_rows = scanned.reshape(GROUP, head_cols) * jax.nn.silu(gate_z.astype(jnp.float32))
    own = jnp.sum(gated_rows * gated_rows, axis=1)
    ways = lax.axis_size("head")
    each = lax.all_to_all(jnp.broadcast_to(own[None], (ways, own.shape[0])), "head", 0, 0, tiled=True)
    squares = each[0]
    for src in range(1, ways):
        squares = squares + each[src]
    scale = lax.rsqrt(squares / (head_cols * lax.axis_size("head")) + EPS)
    return (gated_rows * scale[:, None] * norm_gain[None, :]).astype(jnp.bfloat16)


def solution(mesh):
    seq_size = mesh.shape["seq"]
    grid = Mesh(
        mesh.devices.reshape(seq_size // SEGMENT, SEGMENT, mesh.shape["head"]), ("row", "seg", "head")
    )
    return jax.shard_map(
        body,
        mesh=grid,
        in_specs=(
            P(SEQ, "head"),
            P(SEQ, None),
            P(SEQ, "head"),
            P(SEQ, "head"),
            P(SEQ, "head"),
            P(SEQ),
            P(None, "head"),
            P(),
            P("head"),
            P("head"),
        ),
        out_specs=P(SEQ, "head"),
        check_vma=False,
    )
```

```python
import jax
import jax.numpy as jnp
from jax import lax
from jax.sharding import Mesh
from jax.sharding import PartitionSpec as P

GROUP = 256
SEGMENT = 16


EPS = 1e-05
SEQ = ("row", "seg")


def shifted(block, axis, distance):
    devices = range(lax.axis_size(axis))
    route = [(i - distance, i) for i in devices if i - distance in devices]
    return lax.ppermute(block, axis, route)


def body(x_raw, bc_raw, gate_z, step_size, log_decay, doc_ids, conv_x, conv_bc, skip, norm_gain):
    rows_dev, head_cols = x_raw.shape
    heads_dev = step_size.shape[1]
    head_size = head_cols // heads_dev
    states = bc_raw.shape[1] // 2
    taps = conv_x.shape[0]
    seg = lax.axis_size("seg")
    per_owner = heads_dev // seg
    raw_all = jnp.concatenate([x_raw, bc_raw], axis=1)
    labels = doc_ids + 1
    edge = jnp.concatenate(
        [raw_all[rows_dev - (taps - 1) :], labels[rows_dev - (taps - 1) :, None].astype(jnp.bfloat16)], axis=1
    )
    edge = shifted(edge, SEQ, 1)
    edge_rows = edge[:, : raw_all.shape[1]]
    edge_docs = edge[:, raw_all.shape[1]].astype(jnp.int32)
    extended = jnp.concatenate([edge_rows, raw_all], axis=0)
    ext_docs = jnp.concatenate([edge_docs, labels], axis=0)
    kernel = jnp.concatenate([conv_x, conv_bc], axis=1)
    total = jnp.zeros(raw_all.shape, jnp.float32)
    for k in range(taps):
        moved = extended[taps - 1 - k : taps - 1 - k + rows_dev].astype(jnp.float32)
        keep = (ext_docs[taps - 1 - k : taps - 1 - k + rows_dev] == labels).astype(jnp.float32)
        total = total + kernel[k][None, :] * moved * keep[:, None]
    activated = jax.nn.silu(total).astype(jnp.bfloat16)
    xconv = activated[:, :head_cols].reshape(rows_dev, heads_dev, head_size)
    bconv = activated[:, head_cols : head_cols + states]
    cconv = activated[:, head_cols + states :]
    xdt = (xconv.astype(jnp.float32) * step_size[:, :, None]).astype(jnp.bfloat16)
    lower = jnp.arange(GROUP)[:, None] >= jnp.arange(GROUP)[None, :]
    previous = edge_docs[taps - 2] - 1
    cum = jnp.cumsum(log_decay, axis=0)
    gram = jnp.dot(cconv, bconv.T, preferred_element_type=jnp.float32)
    mask = ((doc_ids[:, None] == doc_ids[None, :]) & lower)[None]
    diff = cum.T[:, :, None] - cum.T[:, None, :]
    weights = (jnp.where(mask, jnp.exp(jnp.where(mask, diff, 0.0)), 0.0) * gram[None]).astype(
        jnp.bfloat16
    )
    inners = jnp.einsum("hts,shp->thp", weights, xdt, preferred_element_type=jnp.float32)
    inners, gate = lax.optimization_barrier((inners, jax.nn.silu(gate_z.astype(jnp.float32))))
    cont = (doc_ids == previous).astype(jnp.float32)
    entries = jnp.exp(cum) * cont[:, None]
    ends = jnp.where((doc_ids == doc_ids[-1])[:, None], jnp.exp(cum[-1][None, :] - cum), 0.0)
    written = (xdt.astype(jnp.float32) * ends[:, :, None]).astype(jnp.bfloat16)
    local = jnp.einsum("shp,sn->hpn", written, bconv, preferred_element_type=jnp.float32)
    through = jnp.exp(cum[-1]) * cont[-1]

    flat = head_size * states
    payload = jnp.concatenate(
        [local.reshape(heads_dev, flat), jnp.broadcast_to(through[:, None], (heads_dev, 128))], axis=1
    )
    got = lax.all_to_all(payload, "seg", 0, 0, tiled=True).reshape(seg, per_owner, flat + 128)
    pieces = jnp.transpose(got[:, :, :flat], (1, 0, 2))
    decays = got[:, :, flat].T
    after = jnp.arange(seg + 1)[:, None, None]
    source = jnp.arange(seg)[None, :, None]
    between = (source < jnp.arange(seg)[None, None, :]) & (jnp.arange(seg)[None, None, :] < after)
    spans = jnp.prod(jnp.where(between[None], decays[:, None, None, :], 1.0), axis=3)
    weights_to = jnp.where((source[..., 0] < after[..., 0])[None], spans, 0.0)
    head_first = jnp.prod(
        jnp.where(jnp.arange(seg)[None, :] < jnp.arange(seg)[:, None], decays[:, None, :], 1.0), axis=2
    )
    exact = lax.Precision.HIGHEST
    total_row = jnp.einsum("gj,gjf->gf", weights_to[:, seg], pieces, precision=exact)
    carry = shifted(total_row, "row", 1)
    folds = jnp.einsum("gij,gjf->gif", weights_to[:, :seg], pieces, precision=exact)
    entering = head_first[:, :, None] * carry[:, None, :] + folds
    entering = jnp.transpose(entering, (1, 0, 2)).reshape(seg, per_owner, head_size, states)
    entered = lax.all_to_all(entering.astype(jnp.bfloat16), "seg", 0, 0, tiled=True).reshape(
        heads_dev, head_size, states
    )

    carried = (
        jnp.einsum("tn,hpn->thp", cconv, entered, preferred_element_type=jnp.float32)
        * entries[:, :, None]
    )
    scanned = inners + carried + skip[None, :, None] * xconv.astype(jnp.float32)
    gated_rows = scanned.reshape(GROUP, head_cols) * gate
    own = jnp.sum(gated_rows * gated_rows, axis=1)
    ways = lax.axis_size("head")
    each = lax.all_to_all(jnp.broadcast_to(own[None], (ways, own.shape[0])), "head", 0, 0, tiled=True)
    squares = each[0]
    for src in range(1, ways):
        squares = squares + each[src]
    scale = lax.rsqrt(squares / (head_cols * lax.axis_size("head")) + EPS)
    return (gated_rows * scale[:, None] * norm_gain[None, :]).astype(jnp.bfloat16)


def solution(mesh):
    seq_size = mesh.shape["seq"]
    grid = Mesh(
        mesh.devices.reshape(seq_size // SEGMENT, SEGMENT, mesh.shape["head"]), ("row", "seg", "head")
    )
    return jax.shard_map(
        body,
        mesh=grid,
        in_specs=(
            P(SEQ, "head"),
            P(SEQ, None),
            P(SEQ, "head"),
            P(SEQ, "head"),
            P(SEQ, "head"),
            P(SEQ),
            P(None, "head"),
            P(),
            P("head"),
            P("head"),
        ),
        out_specs=P(SEQ, "head"),
        check_vma=False,
    )
```

```python
import jax
import jax.numpy as jnp
from jax import lax
from jax.sharding import Mesh
from jax.sharding import PartitionSpec as P

GROUP = 256
SEGMENT = 16


EPS = 1e-05
SEQ = ("row", "seg")


def shifted(block, axis, distance):
    devices = range(lax.axis_size(axis))
    route = [(i - distance, i) for i in devices if i - distance in devices]
    return lax.ppermute(block, axis, route)


def body(x_raw, bc_raw, gate_z, step_size, log_decay, doc_ids, conv_x, conv_bc, skip, norm_gain):
    rows_dev, head_cols = x_raw.shape
    heads_dev = step_size.shape[1]
    head_size = head_cols // heads_dev
    states = bc_raw.shape[1] // 2
    taps = conv_x.shape[0]
    seg = lax.axis_size("seg")
    per_owner = heads_dev // seg
    raw_all = jnp.concatenate([x_raw, bc_raw], axis=1)
    labels = doc_ids + 1
    edge = jnp.concatenate(
        [raw_all[rows_dev - (taps - 1) :], labels[rows_dev - (taps - 1) :, None].astype(jnp.bfloat16)], axis=1
    )
    edge = shifted(edge, SEQ, 1)
    edge_rows = edge[:, : raw_all.shape[1]]
    edge_docs = edge[:, raw_all.shape[1]].astype(jnp.int32)
    extended = jnp.concatenate([edge_rows, raw_all], axis=0)
    ext_docs = jnp.concatenate([edge_docs, labels], axis=0)
    kernel = jnp.concatenate([conv_x, conv_bc], axis=1)
    total = jnp.zeros(raw_all.shape, jnp.float32)
    for k in range(taps):
        moved = extended[taps - 1 - k : taps - 1 - k + rows_dev].astype(jnp.float32)
        keep = (ext_docs[taps - 1 - k : taps - 1 - k + rows_dev] == labels).astype(jnp.float32)
        total = total + kernel[k][None, :] * moved * keep[:, None]
    activated = jax.nn.silu(total).astype(jnp.bfloat16)
    xconv = activated[:, :head_cols].reshape(rows_dev, heads_dev, head_size)
    bconv = activated[:, head_cols : head_cols + states]
    cconv = activated[:, head_cols + states :]
    xdt = (xconv.astype(jnp.float32) * step_size[:, :, None]).astype(jnp.bfloat16)
    lower = jnp.arange(GROUP)[:, None] >= jnp.arange(GROUP)[None, :]
    previous = edge_docs[taps - 2] - 1
    cum = jnp.cumsum(log_decay, axis=0)
    gram = jnp.dot(cconv, bconv.T, preferred_element_type=jnp.float32)
    mask = ((doc_ids[:, None] == doc_ids[None, :]) & lower)[None]
    diff = cum.T[:, :, None] - cum.T[:, None, :]
    weights = (jnp.where(mask, jnp.exp(jnp.where(mask, diff, 0.0)), 0.0) * gram[None]).astype(
        jnp.bfloat16
    )
    inners = jnp.einsum("hts,shp->thp", weights, xdt, preferred_element_type=jnp.float32)
    inners, gate = lax.optimization_barrier((inners, jax.nn.silu(gate_z.astype(jnp.float32))))
    cont = (doc_ids == previous).astype(jnp.float32)
    entries = jnp.exp(cum) * cont[:, None]
    ends = jnp.where((doc_ids == doc_ids[-1])[:, None], jnp.exp(cum[-1][None, :] - cum), 0.0)
    written = (xdt.astype(jnp.float32) * ends[:, :, None]).astype(jnp.bfloat16)
    local = jnp.einsum("shp,sn->hpn", written, bconv, preferred_element_type=jnp.float32)
    through = jnp.where(doc_ids[-1] == previous, jnp.exp(cum[-1]), 0.0)

    flat = head_size * states
    payload = jnp.concatenate(
        [local.reshape(heads_dev, flat), jnp.broadcast_to(through[:, None], (heads_dev, 128))], axis=1
    )
    got = lax.all_to_all(payload, "seg", 0, 0, tiled=True).reshape(seg, per_owner, flat + 128)
    pieces = jnp.transpose(got[:, :, :flat], (1, 0, 2))
    decays = got[:, :, flat].T
    after = jnp.arange(seg + 1)[:, None, None]
    source = jnp.arange(seg)[None, :, None]
    between = (source < jnp.arange(seg)[None, None, :]) & (jnp.arange(seg)[None, None, :] < after)
    spans = jnp.prod(jnp.where(between[None], decays[:, None, None, :], 1.0), axis=3)
    weights_to = jnp.where((source[..., 0] < after[..., 0])[None], spans, 0.0)
    head_first = jnp.prod(
        jnp.where(jnp.arange(seg)[None, :] < jnp.arange(seg)[:, None], decays[:, None, :], 1.0), axis=2
    )
    exact = lax.Precision.HIGHEST
    total_row = jnp.einsum("gj,gjf->gf", weights_to[:, seg], pieces, precision=exact)
    carry = shifted(total_row, "row", 1)
    folds = jnp.einsum("gij,gjf->gif", weights_to[:, :seg], pieces, precision=exact)
    entering = head_first[:, :, None] * carry[:, None, :] + folds
    entering = jnp.transpose(entering, (1, 0, 2)).reshape(seg, per_owner, head_size, states)
    entered = lax.all_to_all(entering.astype(jnp.bfloat16), "seg", 0, 0, tiled=True).reshape(
        heads_dev, head_size, states
    )

    carried = (
        jnp.einsum("tn,hpn->thp", cconv, entered, preferred_element_type=jnp.float32)
        * entries[:, :, None]
    )
    scanned = inners + carried + skip[None, :, None] * xconv.astype(jnp.float32)
    gated_rows = scanned.reshape(GROUP, head_cols) * gate
    own = jnp.sum(gated_rows * gated_rows, axis=1)
    ways = lax.axis_size("head")
    each = lax.all_to_all(jnp.broadcast_to(own[None], (ways, own.shape[0])), "head", 0, 0, tiled=True)
    squares = each[0]
    for src in range(1, ways):
        squares = squares + each[src]
    scale = lax.rsqrt(squares / (head_cols * lax.axis_size("head")) + EPS)
    return (gated_rows * scale[:, None] * norm_gain[None, :]).astype(jnp.bfloat16)


def solution(mesh):
    seq_size = mesh.shape["seq"]
    grid = Mesh(
        mesh.devices.reshape(seq_size // SEGMENT, SEGMENT, mesh.shape["head"]), ("row", "seg", "head")
    )
    return jax.shard_map(
        body,
        mesh=grid,
        in_specs=(
            P(SEQ, "head"),
            P(SEQ, None),
            P(SEQ, "head"),
            P(SEQ, "head"),
            P(SEQ, "head"),
            P(SEQ),
            P(None, "head"),
            P(),
            P("head"),
            P("head"),
        ),
        out_specs=P(SEQ, "head"),
        check_vma=False,
    )
```

```python
import jax
import jax.numpy as jnp
from jax import lax
from jax.sharding import Mesh
from jax.sharding import PartitionSpec as P

GROUP = 256
SEGMENT = 16


EPS = 1e-05
SEQ = ("row", "seg")


def shifted(block, axis, distance):
    devices = range(lax.axis_size(axis))
    route = [(i - distance, i) for i in devices if i - distance in devices]
    return lax.ppermute(block, axis, route)


def body(x_raw, bc_raw, gate_z, step_size, log_decay, doc_ids, conv_x, conv_bc, skip, norm_gain):
    rows_dev, head_cols = x_raw.shape
    heads_dev = step_size.shape[1]
    head_size = head_cols // heads_dev
    states = bc_raw.shape[1] // 2
    taps = conv_x.shape[0]
    seg = lax.axis_size("seg")
    per_owner = heads_dev // seg
    raw_all = jnp.concatenate([x_raw, bc_raw], axis=1)
    labels = doc_ids + 1
    edge = jnp.concatenate(
        [raw_all[rows_dev - (taps - 1) :], labels[rows_dev - (taps - 1) :, None].astype(jnp.bfloat16)], axis=1
    )
    edge = shifted(edge, SEQ, 1)
    edge_rows = edge[:, : raw_all.shape[1]]
    edge_docs = edge[:, raw_all.shape[1]].astype(jnp.int32)
    extended = jnp.concatenate([edge_rows, raw_all], axis=0)
    ext_docs = jnp.concatenate([edge_docs, labels], axis=0)
    kernel = jnp.concatenate([conv_x, conv_bc], axis=1)
    total = jnp.zeros(raw_all.shape, jnp.float32)
    for k in range(taps):
        moved = extended[taps - 1 - k : taps - 1 - k + rows_dev].astype(jnp.float32)
        keep = (ext_docs[taps - 1 - k : taps - 1 - k + rows_dev] == labels).astype(jnp.float32)
        total = total + kernel[k][None, :] * moved * keep[:, None]
    activated = jax.nn.silu(total).astype(jnp.bfloat16)
    xconv = activated[:, :head_cols].reshape(rows_dev, heads_dev, head_size)
    bconv = activated[:, head_cols : head_cols + states]
    cconv = activated[:, head_cols + states :]
    xdt = (xconv.astype(jnp.float32) * step_size[:, :, None]).astype(jnp.bfloat16)
    lower = jnp.arange(GROUP)[:, None] >= jnp.arange(GROUP)[None, :]
    previous = edge_docs[taps - 2] - 1
    cum = jnp.cumsum(log_decay, axis=0)
    gram = jnp.dot(cconv, bconv.T, preferred_element_type=jnp.float32)
    mask = ((doc_ids[:, None] == doc_ids[None, :]) & lower)[None]
    diff = cum.T[:, :, None] - cum.T[:, None, :]
    weights = (jnp.where(mask, jnp.exp(jnp.where(mask, diff, 0.0)), 0.0) * gram[None]).astype(
        jnp.bfloat16
    )
    inners = jnp.einsum("hts,shp->thp", weights, xdt, preferred_element_type=jnp.float32)
    inners, gate = lax.optimization_barrier((inners, jax.nn.silu(gate_z.astype(jnp.float32))))
    cont = (doc_ids == previous).astype(jnp.float32)
    entries = jnp.exp(cum) * cont[:, None]
    last_doc = jnp.max(doc_ids)
    ends = jnp.where((doc_ids == last_doc)[:, None], jnp.exp(cum[-1][None, :] - cum), 0.0)
    written = (xdt.astype(jnp.float32) * ends[:, :, None]).astype(jnp.bfloat16)
    local = jnp.einsum("shp,sn->hpn", written, bconv, preferred_element_type=jnp.float32)
    through = jnp.where(last_doc == previous, jnp.exp(cum[-1]), 0.0)

    flat = head_size * states
    payload = jnp.concatenate(
        [local.reshape(heads_dev, flat), jnp.broadcast_to(through[:, None], (heads_dev, 128))], axis=1
    )
    got = lax.all_to_all(payload, "seg", 0, 0, tiled=True).reshape(seg, per_owner, flat + 128)
    pieces = jnp.transpose(got[:, :, :flat], (1, 0, 2))
    decays = got[:, :, flat].T
    after = jnp.arange(seg + 1)[:, None, None]
    source = jnp.arange(seg)[None, :, None]
    between = (source < jnp.arange(seg)[None, None, :]) & (jnp.arange(seg)[None, None, :] < after)
    spans = jnp.prod(jnp.where(between[None], decays[:, None, None, :], 1.0), axis=3)
    weights_to = jnp.where((source[..., 0] < after[..., 0])[None], spans, 0.0)
    head_first = jnp.prod(
        jnp.where(jnp.arange(seg)[None, :] < jnp.arange(seg)[:, None], decays[:, None, :], 1.0), axis=2
    )
    exact = lax.Precision.HIGHEST
    total_row = jnp.einsum("gj,gjf->gf", weights_to[:, seg], pieces, precision=exact)
    carry = shifted(total_row, "row", 1)
    folds = jnp.einsum("gij,gjf->gif", weights_to[:, :seg], pieces, precision=exact)
    entering = head_first[:, :, None] * carry[:, None, :] + folds
    entering = jnp.transpose(entering, (1, 0, 2)).reshape(seg, per_owner, head_size, states)
    entered = lax.all_to_all(entering.astype(jnp.bfloat16), "seg", 0, 0, tiled=True).reshape(
        heads_dev, head_size, states
    )

    carried = (
        jnp.einsum("tn,hpn->thp", cconv, entered, preferred_element_type=jnp.float32)
        * entries[:, :, None]
    )
    scanned = inners + carried + skip[None, :, None] * xconv.astype(jnp.float32)
    gated_rows = scanned.reshape(GROUP, head_cols) * gate
    own = jnp.sum(gated_rows * gated_rows, axis=1)
    ways = lax.axis_size("head")
    each = lax.all_to_all(jnp.broadcast_to(own[None], (ways, own.shape[0])), "head", 0, 0, tiled=True)
    squares = each[0]
    for src in range(1, ways):
        squares = squares + each[src]
    scale = lax.rsqrt(squares / (head_cols * lax.axis_size("head")) + EPS)
    return (gated_rows * scale[:, None] * norm_gain[None, :]).astype(jnp.bfloat16)


def solution(mesh):
    seq_size = mesh.shape["seq"]
    grid = Mesh(
        mesh.devices.reshape(seq_size // SEGMENT, SEGMENT, mesh.shape["head"]), ("row", "seg", "head")
    )
    return jax.shard_map(
        body,
        mesh=grid,
        in_specs=(
            P(SEQ, "head"),
            P(SEQ, None),
            P(SEQ, "head"),
            P(SEQ, "head"),
            P(SEQ, "head"),
            P(SEQ),
            P(None, "head"),
            P(),
            P("head"),
            P("head"),
        ),
        out_specs=P(SEQ, "head"),
        check_vma=False,
    )
```

```python
import jax
import jax.numpy as jnp
from jax import lax
from jax.sharding import Mesh
from jax.sharding import PartitionSpec as P

GROUP = 256
SEGMENT = 16


EPS = 1e-05
SEQ = ("row", "seg")


def shifted(block, axis, distance):
    devices = range(lax.axis_size(axis))
    route = [(i - distance, i) for i in devices if i - distance in devices]
    return lax.ppermute(block, axis, route)


def body(x_raw, bc_raw, gate_z, step_size, log_decay, doc_ids, conv_x, conv_bc, skip, norm_gain):
    rows_dev, head_cols = x_raw.shape
    heads_dev = step_size.shape[1]
    head_size = head_cols // heads_dev
    states = bc_raw.shape[1] // 2
    taps = conv_x.shape[0]
    seg = lax.axis_size("seg")
    per_owner = heads_dev // seg
    raw_all = jnp.concatenate([x_raw, bc_raw], axis=1)
    labels = doc_ids + 1
    edge = jnp.concatenate(
        [raw_all[rows_dev - (taps - 1) :], labels[rows_dev - (taps - 1) :, None].astype(jnp.bfloat16)], axis=1
    )
    edge = shifted(edge, SEQ, 1)
    edge_rows = edge[:, : raw_all.shape[1]]
    edge_docs = edge[:, raw_all.shape[1]].astype(jnp.int32)
    extended = jnp.concatenate([edge_rows, raw_all], axis=0)
    ext_docs = jnp.concatenate([edge_docs, labels], axis=0)
    kernel = jnp.concatenate([conv_x, conv_bc], axis=1)
    total = jnp.zeros(raw_all.shape, jnp.float32)
    for k in range(taps):
        moved = extended[taps - 1 - k : taps - 1 - k + rows_dev].astype(jnp.float32)
        keep = (ext_docs[taps - 1 - k : taps - 1 - k + rows_dev] == labels).astype(jnp.float32)
        total = total + kernel[k][None, :] * moved * keep[:, None]
    activated = jax.nn.silu(total).astype(jnp.bfloat16)
    xconv = activated[:, :head_cols].reshape(rows_dev, heads_dev, head_size)
    bconv = activated[:, head_cols : head_cols + states]
    cconv = activated[:, head_cols + states :]
    xdt = (xconv.astype(jnp.float32) * step_size[:, :, None]).astype(jnp.bfloat16)
    lower = jnp.arange(GROUP)[:, None] >= jnp.arange(GROUP)[None, :]
    previous = jnp.max(edge_docs) - 1
    cum = jnp.cumsum(log_decay, axis=0)
    gram = jnp.dot(cconv, bconv.T, preferred_element_type=jnp.float32)
    mask = ((doc_ids[:, None] == doc_ids[None, :]) & lower)[None]
    diff = cum.T[:, :, None] - cum.T[:, None, :]
    weights = (jnp.where(mask, jnp.exp(jnp.where(mask, diff, 0.0)), 0.0) * gram[None]).astype(
        jnp.bfloat16
    )
    inners = jnp.einsum("hts,shp->thp", weights, xdt, preferred_element_type=jnp.float32)
    inners, gate = lax.optimization_barrier((inners, jax.nn.silu(gate_z.astype(jnp.float32))))
    cont = (doc_ids == previous).astype(jnp.float32)
    entries = jnp.exp(cum) * cont[:, None]
    ends = jnp.where((doc_ids == doc_ids[-1])[:, None], jnp.exp(cum[-1][None, :] - cum), 0.0)
    written = (xdt.astype(jnp.float32) * ends[:, :, None]).astype(jnp.bfloat16)
    local = jnp.einsum("shp,sn->hpn", written, bconv, preferred_element_type=jnp.float32)
    through = jnp.where(doc_ids[-1] == previous, jnp.exp(cum[-1]), 0.0)

    flat = head_size * states
    payload = jnp.concatenate(
        [local.reshape(heads_dev, flat), jnp.broadcast_to(through[:, None], (heads_dev, 128))], axis=1
    )
    got = lax.all_to_all(payload, "seg", 0, 0, tiled=True).reshape(seg, per_owner, flat + 128)
    pieces = jnp.transpose(got[:, :, :flat], (1, 0, 2))
    decays = got[:, :, flat].T
    after = jnp.arange(seg + 1)[:, None, None]
    source = jnp.arange(seg)[None, :, None]
    between = (source < jnp.arange(seg)[None, None, :]) & (jnp.arange(seg)[None, None, :] < after)
    spans = jnp.prod(jnp.where(between[None], decays[:, None, None, :], 1.0), axis=3)
    weights_to = jnp.where((source[..., 0] < after[..., 0])[None], spans, 0.0)
    head_first = jnp.prod(
        jnp.where(jnp.arange(seg)[None, :] < jnp.arange(seg)[:, None], decays[:, None, :], 1.0), axis=2
    )
    exact = lax.Precision.HIGHEST
    total_row = jnp.einsum("gj,gjf->gf", weights_to[:, seg], pieces, precision=exact)
    carry = shifted(total_row, "row", 1)
    folds = jnp.einsum("gij,gjf->gif", weights_to[:, :seg], pieces, precision=exact)
    entering = head_first[:, :, None] * carry[:, None, :] + folds
    entering = jnp.transpose(entering, (1, 0, 2)).reshape(seg, per_owner, head_size, states)
    entered = lax.all_to_all(entering.astype(jnp.bfloat16), "seg", 0, 0, tiled=True).reshape(
        heads_dev, head_size, states
    )

    carried = (
        jnp.einsum("tn,hpn->thp", cconv, entered, preferred_element_type=jnp.float32)
        * entries[:, :, None]
    )
    scanned = inners + carried + skip[None, :, None] * xconv.astype(jnp.float32)
    gated_rows = scanned.reshape(GROUP, head_cols) * gate
    own = jnp.sum(gated_rows * gated_rows, axis=1)
    ways = lax.axis_size("head")
    each = lax.all_to_all(jnp.broadcast_to(own[None], (ways, own.shape[0])), "head", 0, 0, tiled=True)
    squares = each[0]
    for src in range(1, ways):
        squares = squares + each[src]
    scale = lax.rsqrt(squares / (head_cols * lax.axis_size("head")) + EPS)
    return (gated_rows * scale[:, None] * norm_gain[None, :]).astype(jnp.bfloat16)


def solution(mesh):
    seq_size = mesh.shape["seq"]
    grid = Mesh(
        mesh.devices.reshape(seq_size // SEGMENT, SEGMENT, mesh.shape["head"]), ("row", "seg", "head")
    )
    return jax.shard_map(
        body,
        mesh=grid,
        in_specs=(
            P(SEQ, "head"),
            P(SEQ, None),
            P(SEQ, "head"),
            P(SEQ, "head"),
            P(SEQ, "head"),
            P(SEQ),
            P(None, "head"),
            P(),
            P("head"),
            P("head"),
        ),
        out_specs=P(SEQ, "head"),
        check_vma=False,
    )
```
